128 devices in a mesh: dp: 8 (over y, core), tensor: 16 (over z, x).
Axes of the slice: x: 4, y: 4, z: 4, core: 2. Of those that a mesh axis runs over, the one named last changes fastest.
Arguments:
- features: bfloat16 [1024, 4096], P('dp'), may hold values from -6 to 6
- enc_in: bfloat16 [4096, 2048], P(None, 'tensor'), may hold values from -0.09375 to 0.09375
- enc_out: bfloat16 [2048, 8192], P('tensor'), may hold values from -0.125 to 0.125
- noise: bfloat16 [1024, 4096], P('dp', 'tensor'), may hold values from -6 to 6
- in_weight: bfloat16 [4096, 16384], P('dp', 'tensor'), may hold values from -0.09375 to 0.09375
- out_weight: bfloat16 [4096, 16384], P('dp', 'tensor'), may hold values from -0.046875 to 0.046875
- probes: bfloat16 [2, 1024, 4096], P(None, 'dp'), may hold values from -6 to 6
Outputs:
- flowed: float32 [1024, 4096], P('dp', 'tensor')
- logdet: float32 [1024], P('dp')
The draws below stay inside these ranges and needn't reach their ends.
All inputs are finite; a program needn't handle non-finite values.
Results may differ from the reference program's by a relative error of at most 0.017.
Values may be sent and summed in bfloat16 or wider, within the bound.
No kernel may reach another device: no remote copies, remote signals or barrier semaphores. Data moves between devices by JAX's collectives and lax.ppermute only.
A program may use at most 128 MiB of HBM per device.

```python
import jax
import jax.numpy as jnp

L = 4096
H = 16384
DX = 4096
HE = 2048
PROBES = 2
TERMS = 3
ROWS = 1024


def shard_levels(stream_key, shape, pieces, low, high):
    level, own = 1.0, jax.random.fold_in(stream_key, 6)
    for position, shards_of in pieces:
        draws = jnp.exp(jax.random.uniform(jax.random.fold_in(own, position), (shards_of,), jnp.float32, low / len(pieces), high / len(pieces)))
        level = level * jnp.repeat(draws, shape[position] // shards_of).reshape([-1 if axis == position else 1 for axis in range(len(shape))])
    return level


def centred(stream_key, extent, deviation, limit, shards=(), held_as=jnp.bfloat16):
    loudness = shard_levels(stream_key, extent, shards, -0.22, 0.18) if shards else 1.0
    drawn = jax.random.normal(stream_key, extent, jnp.float32) * deviation * loudness
    return jnp.minimum(jnp.maximum(drawn, -limit), limit).astype(held_as)


def setup_inputs(seed: int = 0) -> dict:
    key_of = jax.random.split(jax.random.key(seed), 8)
    return {
        "features": centred(key_of[0], (ROWS, DX), 1.0, 6.0, ((0, 8),)),
        "enc_in": centred(key_of[1], (DX, HE), DX ** -0.5, 0.09375, ((1, 16),)),
        "enc_out": centred(key_of[2], (HE, 2 * L), HE ** -0.5, 0.125, ((0, 16),)),
        "noise": centred(key_of[3], (ROWS, L), 1.0, 6.0, ((0, 8), (1, 16))),
        "in_weight": centred(key_of[4], (L, H), L ** -0.5, 0.09375, ((0, 8), (1, 16))),
        "out_weight": centred(key_of[5], (L, H), H ** -0.5, 0.046875, ((0, 8), (1, 16))),
        "probes": centred(key_of[6], (PROBES, ROWS, L), 1.0, 6.0, ((1, 8),)),
    }


def reference(features, enc_in, enc_out, noise, in_weight, out_weight, probes):
    hidden = jax.nn.silu(jnp.dot(features, enc_in, preferred_element_type=jnp.float32)).astype(jnp.bfloat16)
    moments = jnp.dot(hidden, enc_out, preferred_element_type=jnp.float32)
    latent = (moments[:, :L] + jax.nn.softplus(moments[:, L:]) * noise.astype(jnp.float32)).astype(jnp.bfloat16)
    pre_act = jnp.dot(latent, in_weight, preferred_element_type=jnp.float32)
    tanh_val = jnp.tanh(pre_act)
    squash = tanh_val.astype(jnp.bfloat16)
    slope = 1.0 - tanh_val * tanh_val
    w_in32 = in_weight.astype(jnp.float32)
    w_out32 = out_weight.astype(jnp.float32)
    branch_sum = jnp.einsum("bh,lh->bl", squash.astype(jnp.float32), w_out32)
    flowed = latent.astype(jnp.float32) + branch_sum
    start32 = probes.astype(jnp.float32)
    current = probes
    running = jnp.zeros((probes.shape[1],), jnp.float32)
    for term_idx in range(TERMS):
        pulled = jnp.einsum("pbl,lh->pbh", current.astype(jnp.float32), w_out32)
        scaled = (pulled * slope[None]).astype(jnp.bfloat16)
        current = jnp.einsum("pbh,lh->pbl", scaled.astype(jnp.float32), w_in32).astype(jnp.bfloat16)
        coeff = (-1.0) ** term_idx / (term_idx + 1)
        running = running + coeff * jnp.sum(start32 * current.astype(jnp.float32), axis=(0, 2))
    logdet = running / PROBES
    return flowed, logdet
```

```python
import jax
import jax.numpy as jnp
from jax import lax
from jax.sharding import PartitionSpec as P

L = 4096
PROBES = 2
TERMS = 3


def collect(partial_value):
    return lax.psum(partial_value.astype(jnp.bfloat16), "tensor")


def gather_dp(block):
    n = lax.axis_size("dp")
    ny = n // 2

    def perm(fn):
        return [(d, fn(d // 2, d % 2)) for d in range(n)]

    up = perm(lambda y, c: 2 * ((y + 1) % ny) + c)
    down = perm(lambda y, c: 2 * ((y - 1) % ny) + c)
    swap = perm(lambda y, c: 2 * y + 1 - c)
    fwd = perm(lambda y, c: 2 * ((y + 1) % ny) if c == 0 else 2 * ((y - 1) % ny) + 1)

    from_below = lax.ppermute(block, "dp", up)
    from_above = lax.ppermute(block, "dp", down)
    partner = lax.ppermute(block, "dp", swap)
    d = lax.axis_index("dp")
    y, c = d // 2, d % 2
    relay = jnp.where(c == 0, from_below, from_above)
    far = lax.ppermute(relay, "dp", fwd)
    partner_near = lax.ppermute(jnp.stack([from_below, from_above]), "dp", swap)
    partner_far = lax.ppermute(far, "dp", swap)
    stacked = jnp.stack(
        [block, partner, from_below, from_above, far, partner_near[0], partner_near[1], partner_far]
    )
    target = jnp.arange(n)
    rel = (target // 2 - y) % ny
    same_pos = jnp.array([0, 3, 4, 2], jnp.int32)[rel]
    other_pos = jnp.array([1, 6, 7, 5], jnp.int32)[rel]
    order = jnp.where(target % 2 == c, same_pos, other_pos)
    return jnp.take(stacked, order, axis=0)


def series(start, w_in, w_out, slope):
    start32 = start.astype(jnp.float32)
    current = start
    running = jnp.zeros((start.shape[1],), jnp.float32)
    for term_idx in range(TERMS):
        pulled = jnp.einsum("pbl,lh->pbh", current, w_out, preferred_element_type=jnp.float32)
        scaled = (pulled * slope[None]).astype(jnp.bfloat16)
        partial_value = jnp.einsum("pbh,lh->pbl", scaled, w_in, preferred_element_type=jnp.float32)
        coeff = (-1.0) ** term_idx / (term_idx + 1)
        if term_idx == TERMS - 1:
            local_dot = jnp.sum(start32 * partial_value, axis=(0, 2))
            running = running + coeff * lax.psum(local_dot, "tensor")
        else:
            current = collect(partial_value)
            running = running + coeff * jnp.sum(start32 * current.astype(jnp.float32), axis=(0, 2))
    return running


def local(features, enc_in, enc_out, noise, in_weight, out_weight, probes):
    rows_here = in_weight.shape[0]
    both = gather_dp(jnp.stack([in_weight, out_weight], axis=0).reshape(2 * rows_here, -1))
    both = both.reshape(-1, 2, rows_here, both.shape[-1])
    w_in = both[:, 0].reshape(-1, both.shape[-1])
    w_out = both[:, 1].reshape(-1, both.shape[-1])
    hidden = jax.nn.silu(jnp.dot(features, enc_in, preferred_element_type=jnp.float32)).astype(
        jnp.bfloat16
    )
    partial_stats = jnp.dot(hidden, enc_out, preferred_element_type=jnp.float32)
    batch_rows = partial_stats.shape[0]
    moments = lax.psum_scatter(
        partial_stats.astype(jnp.bfloat16).reshape(batch_rows, 2, L),
        "tensor",
        scatter_dimension=2,
        tiled=True,
    ).astype(jnp.float32)
    u_slice = (moments[:, 0] + jax.nn.softplus(moments[:, 1]) * noise.astype(jnp.float32)).astype(
        jnp.bfloat16
    )
    u_full = lax.all_gather(u_slice, "tensor", axis=1, tiled=True)
    pre_act = jnp.dot(u_full, w_in, preferred_element_type=jnp.float32)
    tanh_val = jnp.tanh(pre_act)
    squash = tanh_val.astype(jnp.bfloat16)
    slope = 1.0 - tanh_val * tanh_val
    branch_part = jnp.einsum("bh,lh->bl", squash, w_out, preferred_element_type=jnp.float32)
    flowed = u_slice.astype(jnp.float32) + lax.psum_scatter(
        branch_part.astype(jnp.bfloat16), "tensor", scatter_dimension=1, tiled=True
    ).astype(jnp.float32)
    running = series(probes, w_in, w_out, slope)
    logdet = running / PROBES
    return (flowed, logdet)


def solution(mesh):
    in_specs = (
        P("dp", None),
        P(None, "tensor"),
        P("tensor", None),
        P("dp", "tensor"),
        P("dp", "tensor"),
        P("dp", "tensor"),
        P(None, "dp", None),
    )
    out_specs = (P("dp", "tensor"), P("dp"))
    return jax.shard_map(local, mesh=mesh, in_specs=in_specs, out_specs=out_specs, check_vma=False)
```

```python
import jax
import jax.numpy as jnp
from jax import lax
from jax.sharding import PartitionSpec as P

L = 4096
PROBES = 2
TERMS = 3


def gather_dp(block):
    n = lax.axis_size("dp")
    ny = n // 2

    def perm(fn):
        return [(d, fn(d // 2, d % 2)) for d in range(n)]

    up = perm(lambda y, c: 2 * ((y + 1) % ny) + c)
    down = perm(lambda y, c: 2 * ((y - 1) % ny) + c)
    swap = perm(lambda y, c: 2 * y + 1 - c)
    fwd = perm(lambda y, c: 2 * ((y + 1) % ny) if c == 0 else 2 * ((y - 1) % ny) + 1)

    from_below = lax.ppermute(block, "dp", up)
    from_above = lax.ppermute(block, "dp", down)
    partner = lax.ppermute(block, "dp", swap)
    d = lax.axis_index("dp")
    y, c = d // 2, d % 2
    relay = jnp.where(c == 0, from_below, from_above)
    far = lax.ppermute(relay, "dp", fwd)
    partner_near = lax.ppermute(jnp.stack([from_below, from_above]), "dp", swap)
    partner_far = lax.ppermute(far, "dp", swap)
    stacked = jnp.stack(
        [block, partner, from_below, from_above, far, partner_near[0], partner_near[1], partner_far]
    )
    target = jnp.arange(n)
    rel = (target // 2 - y) % ny
    same_pos = jnp.array([0, 3, 4, 2], jnp.int32)[rel]
    other_pos = jnp.array([1, 6, 7, 5], jnp.int32)[rel]
    order = jnp.where(target % 2 == c, same_pos, other_pos)
    return jnp.take(stacked, order, axis=0)


def reduce_scatter_a2a(partial_value, axis):
    n = lax.axis_size("tensor")
    shape = partial_value.shape
    split = shape[:axis] + (n, shape[axis] // n) + shape[axis + 1 :]
    pieces = jnp.moveaxis(partial_value.reshape(split), axis, 0).astype(jnp.bfloat16)
    received = lax.all_to_all(pieces, "tensor", 0, 0)
    return jnp.sum(received.astype(jnp.float32), axis=0)


def all_gather_a2a(piece, axis):
    n = lax.axis_size("tensor")
    sent = jnp.broadcast_to(piece[None], (n,) + piece.shape)
    received = lax.all_to_all(sent, "tensor", 0, 0)
    joined = jnp.moveaxis(received, 0, axis)
    shape = piece.shape
    return joined.reshape(shape[:axis] + (n * shape[axis],) + shape[axis + 1 :])


def psum_butterfly(value):
    n = lax.axis_size("tensor")
    step = 1
    while step < n:
        value = value + lax.ppermute(value, "tensor", [(t, t ^ step) for t in range(n)])
        step *= 2
    return value


def series(start, w_in, w_out, slope):
    n = lax.axis_size("tensor")
    t = lax.axis_index("tensor")
    cols = start.shape[-1] // n
    start32 = start.astype(jnp.float32)
    pulled = jnp.einsum("pbl,lh->pbh", start, w_out, preferred_element_type=jnp.float32)
    scaled = (pulled * slope[None]).astype(jnp.bfloat16)
    pushed = jnp.einsum("pbl,lh->pbh", start, w_in, preferred_element_type=jnp.float32)
    scaled_t = (pushed * slope[None]).astype(jnp.bfloat16)
    part_u = jnp.einsum("pbh,lh->pbl", scaled, w_in, preferred_element_type=jnp.float32)
    part_v = jnp.einsum("pbh,lh->pbl", scaled_t, w_out, preferred_element_type=jnp.float32)
    both = reduce_scatter_a2a(jnp.stack([part_u, part_v]), 3).astype(jnp.bfloat16)
    u_here = both[0].astype(jnp.float32)
    v_here = both[1].astype(jnp.float32)
    start_here = lax.dynamic_slice_in_dim(start32, t * cols, cols, axis=2)
    first = jnp.sum(start_here * u_here, axis=(0, 2))
    second = jnp.sum(v_here * u_here, axis=(0, 2))
    both_full = all_gather_a2a(both, 3)
    u1, v1 = both_full[0], both_full[1]
    pulled3 = jnp.einsum("pbl,lh->pbh", u1, w_out, preferred_element_type=jnp.float32)
    scaled3 = (pulled3 * slope[None]).astype(jnp.bfloat16)
    part3 = jnp.einsum("pbh,lh->pbl", scaled3, w_in, preferred_element_type=jnp.float32)
    third = jnp.sum(v1.astype(jnp.float32) * part3, axis=(0, 2))
    coeffs = [(-1.0) ** k / (k + 1) for k in range(TERMS)]
    local_sum = coeffs[0] * first + coeffs[1] * second + coeffs[2] * third
    return psum_butterfly(local_sum)


def local(features, enc_in, enc_out, noise, in_weight, out_weight, probes):
    w_in = gather_dp(in_weight).reshape(-1, in_weight.shape[-1])
    w_out = gather_dp(out_weight).reshape(-1, out_weight.shape[-1])
    hidden = jax.nn.silu(jnp.dot(features, enc_in, preferred_element_type=jnp.float32)).astype(
        jnp.bfloat16
    )
    partial_stats = jnp.dot(hidden, enc_out, preferred_element_type=jnp.float32)
    batch_rows = partial_stats.shape[0]
    moments = reduce_scatter_a2a(partial_stats.reshape(batch_rows, 2, L), 2)
    u_slice = (moments[:, 0] + jax.nn.softplus(moments[:, 1]) * noise.astype(jnp.float32)).astype(
        jnp.bfloat16
    )
    u_full = all_gather_a2a(u_slice, 1)
    pre_act = jnp.dot(u_full, w_in, preferred_element_type=jnp.float32)
    tanh_val = jnp.tanh(pre_act)
    squash = tanh_val.astype(jnp.bfloat16)
    slope = 1.0 - tanh_val * tanh_val
    branch_part = jnp.einsum("bh,lh->bl", squash, w_out, preferred_element_type=jnp.float32)
    flowed = u_slice.astype(jnp.float32) + lax.psum_scatter(
        branch_part.astype(jnp.bfloat16), "tensor", scatter_dimension=1, tiled=True
    ).astype(jnp.float32)
    running = series(probes, w_in, w_out, slope)
    logdet = running / PROBES
    return (flowed, logdet)


def solution(mesh):
    in_specs = (
        P("dp", None),
        P(None, "tensor"),
        P("tensor", None),
        P("dp", "tensor"),
        P("dp", "tensor"),
        P("dp", "tensor"),
        P(None, "dp", None),
    )
    out_specs = (P("dp", "tensor"), P("dp"))
    return jax.shard_map(local, mesh=mesh, in_specs=in_specs, out_specs=out_specs, check_vma=False)
```

```python
import jax
import jax.numpy as jnp
from jax import lax
from jax.sharding import PartitionSpec as P

L = 4096
PROBES = 2
TERMS = 3


def gather_dp(block):
    n = lax.axis_size("dp")
    ny = n // 2

    def perm(fn):
        return [(d, fn(d // 2, d % 2)) for d in range(n)]

    up = perm(lambda y, c: 2 * ((y + 1) % ny) + c)
    down = perm(lambda y, c: 2 * ((y - 1) % ny) + c)
    swap = perm(lambda y, c: 2 * y + 1 - c)
    fwd = perm(lambda y, c: 2 * ((y + 1) % ny) if c == 0 else 2 * ((y - 1) % ny) + 1)

    from_below = lax.ppermute(block, "dp", up)
    from_above = lax.ppermute(block, "dp", down)
    partner = lax.ppermute(block, "dp", swap)
    d = lax.axis_index("dp")
    y, c = d // 2, d % 2
    relay = jnp.where(c == 0, from_below, from_above)
    far = lax.ppermute(relay, "dp", fwd)
    partner_near = lax.ppermute(jnp.stack([from_below, from_above]), "dp", swap)
    partner_far = lax.ppermute(far, "dp", swap)
    stacked = jnp.stack(
        [block, partner, from_below, from_above, far, partner_near[0], partner_near[1], partner_far]
    )
    target = jnp.arange(n)
    rel = (target // 2 - y) % ny
    same_pos = jnp.array([0, 3, 4, 2], jnp.int32)[rel]
    other_pos = jnp.array([1, 6, 7, 5], jnp.int32)[rel]
    order = jnp.where(target % 2 == c, same_pos, other_pos)
    return jnp.take(stacked, order, axis=0)


def reduce_scatter_pieces(pieces):
    received = lax.all_to_all(pieces.astype(jnp.bfloat16), "tensor", 0, 0)
    return jnp.sum(received.astype(jnp.float32), axis=0)


def all_gather_pieces(piece):
    n = lax.axis_size("tensor")
    return lax.all_to_all(jnp.broadcast_to(piece[None], (n,) + piece.shape), "tensor", 0, 0)


def psum_butterfly(value):
    n = lax.axis_size("tensor")
    step = 1
    while step < n:
        value = value + lax.ppermute(value, "tensor", [(t, t ^ step) for t in range(n)])
        step *= 2
    return value


def series(start, w_in_p, w_out_p, slope, side):
    n, cols = w_in_p.shape[0], w_in_p.shape[1]
    t = lax.axis_index("tensor")
    start_p = start.reshape(start.shape[0], start.shape[1], n, cols)
    pulled = jnp.einsum("pbsc,sch->pbh", start_p, w_out_p, preferred_element_type=jnp.float32)
    scaled = (pulled * slope[None]).astype(jnp.bfloat16)
    part_u = jnp.einsum("pbh,sch->spbc", scaled, w_in_p, preferred_element_type=jnp.float32)
    with_side = reduce_scatter_pieces(jnp.concatenate([part_u, side[:, None]], axis=1))
    u_here = with_side[:-1].astype(jnp.bfloat16)
    side = with_side[-1]
    pushed = jnp.einsum("pbsc,sch->pbh", start_p, w_in_p, preferred_element_type=jnp.float32)
    scaled_t = (pushed * slope[None]).astype(jnp.bfloat16)
    part_v = jnp.einsum("pbh,sch->spbc", scaled_t, w_out_p, preferred_element_type=jnp.float32)
    v_here = reduce_scatter_pieces(part_v).astype(jnp.bfloat16)
    u_pieces = all_gather_pieces(u_here)
    v_pieces = all_gather_pieces(v_here)
    start_here = lax.dynamic_index_in_dim(start_p, t, axis=2, keepdims=False).astype(jnp.float32)
    first = jnp.sum(start_here * u_here.astype(jnp.float32), axis=(0, 2))
    second = jnp.sum(v_here.astype(jnp.float32) * u_here.astype(jnp.float32), axis=(0, 2))
    pulled3 = jnp.einsum("spbc,sch->pbh", u_pieces, w_out_p, preferred_element_type=jnp.float32)
    scaled3 = (pulled3 * slope[None]).astype(jnp.bfloat16)
    part3 = jnp.einsum("pbh,sch->spbc", scaled3, w_in_p, preferred_element_type=jnp.float32)
    third = jnp.sum(v_pieces.astype(jnp.float32) * part3, axis=(0, 1, 3))
    coeffs = [(-1.0) ** k / (k + 1) for k in range(TERMS)]
    local_sum = coeffs[0] * first + coeffs[1] * second + coeffs[2] * third
    return psum_butterfly(local_sum), side


def local(features, enc_in, enc_out, noise, in_weight, out_weight, probes):
    n = lax.axis_size("tensor")
    w_in = gather_dp(in_weight).reshape(n, -1, in_weight.shape[-1])
    w_out = gather_dp(out_weight).reshape(n, -1, out_weight.shape[-1])
    hidden = jax.nn.silu(jnp.dot(features, enc_in, preferred_element_type=jnp.float32)).astype(
        jnp.bfloat16
    )
    enc_out_p = enc_out.reshape(enc_out.shape[0], 2, n, -1)
    stats_p = jnp.einsum("bk,kmsc->sbmc", hidden, enc_out_p, preferred_element_type=jnp.float32)
    moments = reduce_scatter_pieces(stats_p)
    u_slice = (moments[:, 0] + jax.nn.softplus(moments[:, 1]) * noise.astype(jnp.float32)).astype(
        jnp.bfloat16
    )
    u_pieces = all_gather_pieces(u_slice)
    pre_act = jnp.einsum("sbc,sch->bh", u_pieces, w_in, preferred_element_type=jnp.float32)
    tanh_val = jnp.tanh(pre_act)
    squash = tanh_val.astype(jnp.bfloat16)
    slope = 1.0 - tanh_val * tanh_val
    branch_part = jnp.einsum("bh,sch->sbc", squash, w_out, preferred_element_type=jnp.float32)
    running, branch = series(probes, w_in, w_out, slope, branch_part)
    flowed = u_slice.astype(jnp.float32) + branch
    logdet = running / PROBES
    return (flowed, logdet)


def solution(mesh):
    in_specs = (
        P("dp", None),
        P(None, "tensor"),
        P("tensor", None),
        P("dp", "tensor"),
        P("dp", "tensor"),
        P("dp", "tensor"),
        P(None, "dp", None),
    )
    out_specs = (P("dp", "tensor"), P("dp"))
    return jax.shard_map(local, mesh=mesh, in_specs=in_specs, out_specs=out_specs, check_vma=False)
```

```python
import jax
import jax.numpy as jnp
from jax import lax
from jax.sharding import PartitionSpec as P

L = 4096
PROBES = 2
TERMS = 3


def gather_dp(block):
    n = lax.axis_size("dp")
    ny = n // 2

    def perm(fn):
        return [(d, fn(d // 2, d % 2)) for d in range(n)]

    up = perm(lambda y, c: 2 * ((y + 1) % ny) + c)
    down = perm(lambda y, c: 2 * ((y - 1) % ny) + c)
    swap = perm(lambda y, c: 2 * y + 1 - c)
    fwd = perm(lambda y, c: 2 * ((y + 1) % ny) if c == 0 else 2 * ((y - 1) % ny) + 1)

    from_below = lax.ppermute(block, "dp", up)
    from_above = lax.ppermute(block, "dp", down)
    partner = lax.ppermute(block, "dp", swap)
    d = lax.axis_index("dp")
    y, c = d // 2, d % 2
    relay = jnp.where(c == 0, from_below, from_above)
    far = lax.ppermute(relay, "dp", fwd)
    partner_near = lax.ppermute(jnp.stack([from_below, from_above]), "dp", swap)
    partner_far = lax.ppermute(far, "dp", swap)
    joined = jnp.concatenate(
        [block, partner, from_below, from_above, far, partner_near[0], partner_near[1], partner_far]
    )
    rel_y = jnp.array([0, 0, -1, 1, 2, -1, 1, 2], jnp.int32)
    flip = jnp.array([0, 1, 0, 0, 0, 1, 1, 1], jnp.int32)
    block_ids = 2 * ((y + rel_y) % ny) + (c ^ flip)
    return joined, block_ids


def reduce_scatter_pieces(pieces):
    received = lax.all_to_all(pieces.astype(jnp.bfloat16), "tensor", 0, 0)
    return jnp.sum(received.astype(jnp.float32), axis=0)


def all_gather_pieces(piece):
    n = lax.axis_size("tensor")
    return lax.all_to_all(jnp.broadcast_to(piece[None], (n,) + piece.shape), "tensor", 0, 0)


def psum_groups(value):
    n = lax.axis_size("tensor")
    step = 1
    while step < n:
        others = [lax.ppermute(value, "tensor", [(t, t ^ (k * step)) for t in range(n)]) for k in (1, 2, 3)]
        value = (value + others[0]) + (others[1] + others[2])
        step *= 4
    return value


def series(start_p, w_in_p, w_out_p, slope, side):
    t = lax.axis_index("tensor")
    pulled = jnp.einsum("pbsc,sch->pbh", start_p, w_out_p, preferred_element_type=jnp.float32)
    scaled = (pulled * slope[None]).astype(jnp.bfloat16)
    part_u = jnp.einsum("pbh,sch->spbc", scaled, w_in_p, preferred_element_type=jnp.float32)
    pushed = jnp.einsum("pbsc,sch->pbh", start_p, w_in_p, preferred_element_type=jnp.float32)
    scaled_t = (pushed * slope[None]).astype(jnp.bfloat16)
    part_v = jnp.einsum("pbh,sch->spbc", scaled_t, w_out_p, preferred_element_type=jnp.float32)
    summed = reduce_scatter_pieces(jnp.concatenate([part_u, part_v, side[:, None]], axis=1))
    probes_n = start_p.shape[0]
    uv_here = summed[: 2 * probes_n].astype(jnp.bfloat16)
    side = summed[2 * probes_n]
    u_here = uv_here[:probes_n].astype(jnp.float32)
    v_here = uv_here[probes_n:].astype(jnp.float32)
    uv_pieces = all_gather_pieces(uv_here)
    start_here = lax.dynamic_index_in_dim(start_p, t, axis=2, keepdims=False).astype(jnp.float32)
    first = jnp.sum(start_here * u_here, axis=(0, 2))
    second = jnp.sum(v_here * u_here, axis=(0, 2))
    pulled3 = jnp.einsum(
        "spbc,sch->pbh", uv_pieces[:, :probes_n], w_out_p, preferred_element_type=jnp.float32
    )
    scaled3 = (pulled3 * slope[None]).astype(jnp.bfloat16)
    part3 = jnp.einsum("pbh,sch->spbc", scaled3, w_in_p, preferred_element_type=jnp.float32)
    third = jnp.sum(uv_pieces[:, probes_n:].astype(jnp.float32) * part3, axis=(0, 1, 3))
    coeffs = [(-1.0) ** k / (k + 1) for k in range(TERMS)]
    local_sum = coeffs[0] * first + coeffs[1] * second + coeffs[2] * third
    return psum_groups(local_sum), side


def local(features, enc_in, enc_out, noise, in_weight, out_weight, probes):
    n = lax.axis_size("tensor")
    w_in, block_ids = gather_dp(in_weight)
    w_out, _ = gather_dp(out_weight)
    w_in = w_in.reshape(n, -1, in_weight.shape[-1])
    w_out = w_out.reshape(n, -1, out_weight.shape[-1])
    halves = n // block_ids.shape[0]
    order = (halves * block_ids[:, None] + jnp.arange(halves)[None, :]).reshape(-1)
    back = jnp.argsort(order)
    hidden = jax.nn.silu(jnp.dot(features, enc_in, preferred_element_type=jnp.float32)).astype(
        jnp.bfloat16
    )
    enc_out_p = enc_out.reshape(enc_out.shape[0], 2, n, -1)
    stats_p = jnp.einsum("bk,kmsc->sbmc", hidden, enc_out_p, preferred_element_type=jnp.float32)
    moments = reduce_scatter_pieces(stats_p)
    u_slice = (moments[:, 0] + jax.nn.softplus(moments[:, 1]) * noise.astype(jnp.float32)).astype(
        jnp.bfloat16
    )
    u_pieces = jnp.take(all_gather_pieces(u_slice), order, axis=0, mode="clip")
    pre_act = jnp.einsum("sbc,sch->bh", u_pieces, w_in, preferred_element_type=jnp.float32)
    tanh_val = jnp.tanh(pre_act)
    squash = tanh_val.astype(jnp.bfloat16)
    slope = 1.0 - tanh_val * tanh_val
    branch_part = jnp.einsum("bh,sch->sbc", squash, w_out, preferred_element_type=jnp.float32)
    branch_part = jnp.take(branch_part, back, axis=0, mode="clip")
    start_p = probes.reshape(probes.shape[0], probes.shape[1], n, -1)
    start_p = jnp.take(start_p, order, axis=2, mode="clip")
    running, branch = series(start_p, w_in, w_out, slope, branch_part)
    flowed = u_slice.astype(jnp.float32) + branch
    logdet = running / PROBES
    return (flowed, logdet)


def solution(mesh):
    in_specs = (
        P("dp", None),
        P(None, "tensor"),
        P("tensor", None),
        P("dp", "tensor"),
        P("dp", "tensor"),
        P("dp", "tensor"),
        P(None, "dp", None),
    )
    out_specs = (P("dp", "tensor"), P("dp"))
    return jax.shard_map(local, mesh=mesh, in_specs=in_specs, out_specs=out_specs, check_vma=False)
```

```python
import jax
import jax.numpy as jnp
from jax import lax
from jax.sharding import PartitionSpec as P

L = 4096
PROBES = 2
TERMS = 3


def gather_dp(block):
    n = lax.axis_size("dp")
    ny = n // 2

    def perm(fn):
        return [(d, fn(d // 2, d % 2)) for d in range(n)]

    up = perm(lambda y, c: 2 * ((y + 1) % ny) + c)
    down = perm(lambda y, c: 2 * ((y - 1) % ny) + c)
    swap = perm(lambda y, c: 2 * y + 1 - c)
    fwd = perm(lambda y, c: 2 * ((y + 1) % ny) if c == 0 else 2 * ((y - 1) % ny) + 1)

    from_below = lax.ppermute(block, "dp", up)
    from_above = lax.ppermute(block, "dp", down)
    partner = lax.ppermute(block, "dp", swap)
    d = lax.axis_index("dp")
    y, c = d // 2, d % 2
    relay = jnp.where(c == 0, from_below, from_above)
    far = lax.ppermute(relay, "dp", fwd)
    partner_near = lax.ppermute(jnp.stack([from_below, from_above]), "dp", swap)
    partner_far = lax.ppermute(far, "dp", swap)
    joined = jnp.concatenate(
        [block, partner, from_below, from_above, far, partner_near[0], partner_near[1], partner_far]
    )
    rel_y = jnp.array([0, 0, -1, 1, 2, -1, 1, 2], jnp.int32)
    flip = jnp.array([0, 1, 0, 0, 0, 1, 1, 1], jnp.int32)
    block_ids = 2 * ((y + rel_y) % ny) + (c ^ flip)
    return joined, block_ids


def reduce_scatter_pieces(pieces):
    received = lax.all_to_all(pieces.astype(jnp.bfloat16), "tensor", 0, 0)
    return jnp.sum(received.astype(jnp.float32), axis=0)


def all_gather_pieces(piece):
    n = lax.axis_size("tensor")
    return lax.all_to_all(jnp.broadcast_to(piece[None], (n,) + piece.shape), "tensor", 0, 0)


def psum_groups(value):
    n = lax.axis_size("tensor")
    step = 1
    while step < n:
        others = [lax.ppermute(value, "tensor", [(t, t ^ (k * step)) for t in range(n)]) for k in (1, 2, 3)]
        value = (value + others[0]) + (others[1] + others[2])
        step *= 4
    return value


def series(start_p, order, w_in_p, w_out_p, slope, side):
    t = lax.axis_index("tensor")
    back = jnp.argsort(order)
    start_in = jnp.take(start_p, order, axis=2, mode="clip")
    pulled = jnp.einsum("pbsc,sch->pbh", start_p, w_out_p, preferred_element_type=jnp.float32)
    scaled = (pulled * slope[None]).astype(jnp.bfloat16)
    part_u = jnp.einsum("pbh,sch->spbc", scaled, w_in_p, preferred_element_type=jnp.float32)
    part_u = jnp.take(part_u, back, axis=0, mode="clip")
    pushed = jnp.einsum("pbsc,sch->pbh", start_in, w_in_p, preferred_element_type=jnp.float32)
    scaled_t = (pushed * slope[None]).astype(jnp.bfloat16)
    part_v = jnp.einsum("pbh,sch->spbc", scaled_t, w_out_p, preferred_element_type=jnp.float32)
    summed = reduce_scatter_pieces(jnp.concatenate([part_u, part_v, side[:, None]], axis=1))
    probes_n = start_p.shape[0]
    uv_here = summed[: 2 * probes_n].astype(jnp.bfloat16)
    side = summed[2 * probes_n]
    u_here = uv_here[:probes_n].astype(jnp.float32)
    v_here = uv_here[probes_n:].astype(jnp.float32)
    uv_pieces = all_gather_pieces(uv_here)
    start_here = lax.dynamic_index_in_dim(start_p, t, axis=2, keepdims=False).astype(jnp.float32)
    first = jnp.sum(start_here * u_here, axis=(0, 2))
    second = jnp.sum(v_here * u_here, axis=(0, 2))
    pulled3 = jnp.einsum(
        "spbc,sch->pbh", uv_pieces[:, :probes_n], w_out_p, preferred_element_type=jnp.float32
    )
    scaled3 = (pulled3 * slope[None]).astype(jnp.bfloat16)
    part3 = jnp.einsum("pbh,sch->spbc", scaled3, w_in_p, preferred_element_type=jnp.float32)
    v_in = jnp.take(uv_pieces[:, probes_n:], order, axis=0, mode="clip")
    third = jnp.sum(v_in.astype(jnp.float32) * part3, axis=(0, 1, 3))
    coeffs = [(-1.0) ** k / (k + 1) for k in range(TERMS)]
    local_sum = coeffs[0] * first + coeffs[1] * second + coeffs[2] * third
    return psum_groups(local_sum), side


def local(features, enc_in, enc_out, noise, in_weight, out_weight, probes):
    n = lax.axis_size("tensor")
    w_in, block_ids = gather_dp(in_weight)
    w_in = w_in.reshape(n, -1, in_weight.shape[-1])
    w_out = lax.all_gather(out_weight, "dp", axis=0, tiled=True).reshape(n, -1, out_weight.shape[-1])
    halves = n // block_ids.shape[0]
    order = (halves * block_ids[:, None] + jnp.arange(halves)[None, :]).reshape(-1)
    hidden = jax.nn.silu(jnp.dot(features, enc_in, preferred_element_type=jnp.float32)).astype(
        jnp.bfloat16
    )
    enc_out_p = enc_out.reshape(enc_out.shape[0], 2, n, -1)
    stats_p = jnp.einsum("bk,kmsc->sbmc", hidden, enc_out_p, preferred_element_type=jnp.float32)
    moments = reduce_scatter_pieces(stats_p)
    u_slice = (moments[:, 0] + jax.nn.softplus(moments[:, 1]) * noise.astype(jnp.float32)).astype(
        jnp.bfloat16
    )
    u_pieces = jnp.take(all_gather_pieces(u_slice), order, axis=0, mode="clip")
    pre_act = jnp.einsum("sbc,sch->bh", u_pieces, w_in, preferred_element_type=jnp.float32)
    tanh_val = jnp.tanh(pre_act)
    squash = tanh_val.astype(jnp.bfloat16)
    slope = 1.0 - tanh_val * tanh_val
    branch_part = jnp.einsum("bh,sch->sbc", squash, w_out, preferred_element_type=jnp.float32)
    start_p = probes.reshape(probes.shape[0], probes.shape[1], n, -1)
    running, branch = series(start_p, order, w_in, w_out, slope, branch_part)
    flowed = u_slice.astype(jnp.float32) + branch
    logdet = running / PROBES
    return (flowed, logdet)


def solution(mesh):
    in_specs = (
        P("dp", None),
        P(None, "tensor"),
        P("tensor", None),
        P("dp", "tensor"),
        P("dp", "tensor"),
        P("dp", "tensor"),
        P(None, "dp", None),
    )
    out_specs = (P("dp", "tensor"), P("dp"))
    return jax.shard_map(local, mesh=mesh, in_specs=in_specs, out_specs=out_specs, check_vma=False)
```

```python
import jax
import jax.numpy as jnp
from jax import lax
from jax.sharding import PartitionSpec as P

L = 4096
PROBES = 2
TERMS = 3


def gather_dp(block, after=None):
    n = lax.axis_size("dp")
    ny = n // 2
    if after is not None:
        block, _ = lax.optimization_barrier((block, after))

    def perm(fn):
        return [(d, fn(d // 2, d % 2)) for d in range(n)]

    up = perm(lambda y, c: 2 * ((y + 1) % ny) + c)
    down = perm(lambda y, c: 2 * ((y - 1) % ny) + c)
    swap = perm(lambda y, c: 2 * y + 1 - c)
    fwd = perm(lambda y, c: 2 * ((y + 1) % ny) if c == 0 else 2 * ((y - 1) % ny) + 1)

    from_below = lax.ppermute(block, "dp", up)
    from_above = lax.ppermute(block, "dp", down)
    partner = lax.ppermute(block, "dp", swap)
    d = lax.axis_index("dp")
    y, c = d // 2, d % 2
    relay = jnp.where(c == 0, from_below, from_above)
    far = lax.ppermute(relay, "dp", fwd)
    partner_near = lax.ppermute(jnp.stack([from_below, from_above]), "dp", swap)
    partner_far = lax.ppermute(far, "dp", swap)
    joined = jnp.concatenate(
        [block, partner, from_below, from_above, far, partner_near[0], partner_near[1], partner_far]
    )
    rel_y = jnp.array([0, 0, -1, 1, 2, -1, 1, 2], jnp.int32)
    flip = jnp.array([0, 1, 0, 0, 0, 1, 1, 1], jnp.int32)
    block_ids = 2 * ((y + rel_y) % ny) + (c ^ flip)
    return joined, block_ids, (from_below, from_above, far)


def reduce_scatter_pieces(pieces):
    received = lax.all_to_all(pieces.astype(jnp.bfloat16), "tensor", 0, 0)
    return jnp.sum(received.astype(jnp.float32), axis=0)


def all_gather_pieces(piece):
    n = lax.axis_size("tensor")
    return lax.all_to_all(jnp.broadcast_to(piece[None], (n,) + piece.shape), "tensor", 0, 0)


def psum_groups(value):
    n = lax.axis_size("tensor")
    step = 1
    while step < n:
        others = [lax.ppermute(value, "tensor", [(t, t ^ (k * step)) for t in range(n)]) for k in (1, 2, 3)]
        value = (value + others[0]) + (others[1] + others[2])
        step *= 4
    return value


def series(start_p, w_in_p, w_out_p, slope, side):
    t = lax.axis_index("tensor")
    pulled = jnp.einsum("pbsc,sch->pbh", start_p, w_out_p, preferred_element_type=jnp.float32)
    scaled = (pulled * slope[None]).astype(jnp.bfloat16)
    part_u = jnp.einsum("pbh,sch->spbc", scaled, w_in_p, preferred_element_type=jnp.float32)
    pushed = jnp.einsum("pbsc,sch->pbh", start_p, w_in_p, preferred_element_type=jnp.float32)
    scaled_t = (pushed * slope[None]).astype(jnp.bfloat16)
    part_v = jnp.einsum("pbh,sch->spbc", scaled_t, w_out_p, preferred_element_type=jnp.float32)
    summed = reduce_scatter_pieces(jnp.concatenate([part_u, part_v, side[:, None]], axis=1))
    probes_n = start_p.shape[0]
    uv_here = summed[: 2 * probes_n].astype(jnp.bfloat16)
    side = summed[2 * probes_n]
    u_here = uv_here[:probes_n].astype(jnp.float32)
    v_here = uv_here[probes_n:].astype(jnp.float32)
    uv_pieces = all_gather_pieces(uv_here)
    start_here = lax.dynamic_index_in_dim(start_p, t, axis=2, keepdims=False).astype(jnp.float32)
    first = jnp.sum(start_here * u_here, axis=(0, 2))
    second = jnp.sum(v_here * u_here, axis=(0, 2))
    pulled3 = jnp.einsum(
        "spbc,sch->pbh", uv_pieces[:, :probes_n], w_out_p, preferred_element_type=jnp.float32
    )
    scaled3 = (pulled3 * slope[None]).astype(jnp.bfloat16)
    part3 = jnp.einsum("pbh,sch->spbc", scaled3, w_in_p, preferred_element_type=jnp.float32)
    third = jnp.sum(uv_pieces[:, probes_n:].astype(jnp.float32) * part3, axis=(0, 1, 3))
    coeffs = [(-1.0) ** k / (k + 1) for k in range(TERMS)]
    local_sum = coeffs[0] * first + coeffs[1] * second + coeffs[2] * third
    return psum_groups(local_sum), side


def local(features, enc_in, enc_out, noise, in_weight, out_weight, probes):
    n = lax.axis_size("tensor")
    w_in, block_ids, first_round = gather_dp(in_weight)
    w_out, _, _ = gather_dp(out_weight, after=first_round)
    w_in = w_in.reshape(n, -1, in_weight.shape[-1])
    w_out = w_out.reshape(n, -1, out_weight.shape[-1])
    halves = n // block_ids.shape[0]
    order = (halves * block_ids[:, None] + jnp.arange(halves)[None, :]).reshape(-1)
    back = jnp.argsort(order)
    hidden = jax.nn.silu(jnp.dot(features, enc_in, preferred_element_type=jnp.float32)).astype(
        jnp.bfloat16
    )
    enc_out_p = enc_out.reshape(enc_out.shape[0], 2, n, -1)
    stats_p = jnp.einsum("bk,kmsc->sbmc", hidden, enc_out_p, preferred_element_type=jnp.float32)
    moments = reduce_scatter_pieces(stats_p)
    u_slice = (moments[:, 0] + jax.nn.softplus(moments[:, 1]) * noise.astype(jnp.float32)).astype(
        jnp.bfloat16
    )
    u_pieces = jnp.take(all_gather_pieces(u_slice), order, axis=0, mode="clip")
    pre_act = jnp.einsum("sbc,sch->bh", u_pieces, w_in, preferred_element_type=jnp.float32)
    tanh_val = jnp.tanh(pre_act)
    squash = tanh_val.astype(jnp.bfloat16)
    slope = 1.0 - tanh_val * tanh_val
    branch_part = jnp.einsum("bh,sch->sbc", squash, w_out, preferred_element_type=jnp.float32)
    branch_part = jnp.take(branch_part, back, axis=0, mode="clip")
    start_p = probes.reshape(probes.shape[0], probes.shape[1], n, -1)
    start_p = jnp.take(start_p, order, axis=2, mode="clip")
    running, branch = series(start_p, w_in, w_out, slope, branch_part)
    flowed = u_slice.astype(jnp.float32) + branch
    logdet = running / PROBES
    return (flowed, logdet)


def solution(mesh):
    in_specs = (
        P("dp", None),
        P(None, "tensor"),
        P("tensor", None),
        P("dp", "tensor"),
        P("dp", "tensor"),
        P("dp", "tensor"),
        P(None, "dp", None),
    )
    out_specs = (P("dp", "tensor"), P("dp"))
    return jax.shard_map(local, mesh=mesh, in_specs=in_specs, out_specs=out_specs, check_vma=False)
```

```python
import jax
import jax.numpy as jnp
from jax import lax
from jax.sharding import PartitionSpec as P

L = 4096
PROBES = 2
TERMS = 3


def gather_dp(block):
    n = lax.axis_size("dp")
    ny = n // 2

    def perm(fn):
        return [(d, fn(d // 2, d % 2)) for d in range(n)]

    up = perm(lambda y, c: 2 * ((y + 1) % ny) + c)
    down = perm(lambda y, c: 2 * ((y - 1) % ny) + c)
    swap = perm(lambda y, c: 2 * y + 1 - c)
    fwd = perm(lambda y, c: 2 * ((y + 1) % ny) if c == 0 else 2 * ((y - 1) % ny) + 1)

    from_below = lax.ppermute(block, "dp", up)
    from_above = lax.ppermute(block, "dp", down)
    partner = lax.ppermute(block, "dp", swap)
    d = lax.axis_index("dp")
    y, c = d // 2, d % 2
    relay = jnp.where(c == 0, from_below, from_above)
    far = lax.ppermute(relay, "dp", fwd)
    partner_near = lax.ppermute(jnp.stack([from_below, from_above]), "dp", swap)
    partner_far = lax.ppermute(far, "dp", swap)
    joined = jnp.concatenate(
        [block, partner, from_below, from_above, far, partner_near[0], partner_near[1], partner_far]
    )
    rel_y = jnp.array([0, 0, -1, 1, 2, -1, 1, 2], jnp.int32)
    flip = jnp.array([0, 1, 0, 0, 0, 1, 1, 1], jnp.int32)
    block_ids = 2 * ((y + rel_y) % ny) + (c ^ flip)
    return joined, block_ids


def reduce_scatter_pieces(pieces):
    received = lax.all_to_all(pieces.astype(jnp.bfloat16), "tensor", 0, 0)
    return jnp.sum(received.astype(jnp.float32), axis=0)


def all_gather_pieces(piece):
    n = lax.axis_size("tensor")
    return lax.all_to_all(jnp.broadcast_to(piece[None], (n,) + piece.shape), "tensor", 0, 0)


def psum_groups(value):
    n = lax.axis_size("tensor")
    step = 1
    while step < n:
        others = [lax.ppermute(value, "tensor", [(t, t ^ (k * step)) for t in range(n)]) for k in (1, 2, 3)]
        value = (value + others[0]) + (others[1] + others[2])
        step *= 4
    return value


def series(start_p, w_in_p, w_out_p, slope, side):
    t = lax.axis_index("tensor")
    pulled = jnp.einsum("pbsc,sch->pbh", start_p, w_out_p, preferred_element_type=jnp.float32)
    scaled = (pulled * slope[None]).astype(jnp.bfloat16)
    part_u = jnp.einsum("pbh,sch->spbc", scaled, w_in_p, preferred_element_type=jnp.float32)
    pushed = jnp.einsum("pbsc,sch->pbh", start_p, w_in_p, preferred_element_type=jnp.float32)
    scaled_t = (pushed * slope[None]).astype(jnp.bfloat16)
    part_v = jnp.einsum("pbh,sch->spbc", scaled_t, w_out_p, preferred_element_type=jnp.float32)
    summed = reduce_scatter_pieces(jnp.concatenate([part_u, part_v, side[:, None]], axis=1))
    probes_n = start_p.shape[0]
    uv_here = summed[: 2 * probes_n].astype(jnp.bfloat16)
    side = summed[2 * probes_n]
    u_here = uv_here[:probes_n].astype(jnp.float32)
    v_here = uv_here[probes_n:].astype(jnp.float32)
    u_pieces = all_gather_pieces(uv_here[:probes_n])
    v_pieces = lax.all_gather(uv_here[probes_n:], "tensor", axis=0, tiled=False)
    start_here = lax.dynamic_index_in_dim(start_p, t, axis=2, keepdims=False).astype(jnp.float32)
    first = jnp.sum(start_here * u_here, axis=(0, 2))
    second = jnp.sum(v_here * u_here, axis=(0, 2))
    pulled3 = jnp.einsum(
        "spbc,sch->pbh", u_pieces, w_out_p, preferred_element_type=jnp.float32
    )
    scaled3 = (pulled3 * slope[None]).astype(jnp.bfloat16)
    part3 = jnp.einsum("pbh,sch->spbc", scaled3, w_in_p, preferred_element_type=jnp.float32)
    third = jnp.sum(v_pieces.astype(jnp.float32) * part3, axis=(0, 1, 3))
    coeffs = [(-1.0) ** k / (k + 1) for k in range(TERMS)]
    local_sum = coeffs[0] * first + coeffs[1] * second + coeffs[2] * third
    return psum_groups(local_sum), side


def local(features, enc_in, enc_out, noise, in_weight, out_weight, probes):
    n = lax.axis_size("tensor")
    w_in, block_ids = gather_dp(in_weight)
    w_out, _ = gather_dp(out_weight)
    w_in = w_in.reshape(n, -1, in_weight.shape[-1])
    w_out = w_out.reshape(n, -1, out_weight.shape[-1])
    halves = n // block_ids.shape[0]
    order = (halves * block_ids[:, None] + jnp.arange(halves)[None, :]).reshape(-1)
    back = jnp.argsort(order)
    hidden = jax.nn.silu(jnp.dot(features, enc_in, preferred_element_type=jnp.float32)).astype(
        jnp.bfloat16
    )
    enc_out_p = enc_out.reshape(enc_out.shape[0], 2, n, -1)
    stats_p = jnp.einsum("bk,kmsc->sbmc", hidden, enc_out_p, preferred_element_type=jnp.float32)
    moments = reduce_scatter_pieces(stats_p)
    u_slice = (moments[:, 0] + jax.nn.softplus(moments[:, 1]) * noise.astype(jnp.float32)).astype(
        jnp.bfloat16
    )
    u_pieces = jnp.take(all_gather_pieces(u_slice), order, axis=0, mode="clip")
    pre_act = jnp.einsum("sbc,sch->bh", u_pieces, w_in, preferred_element_type=jnp.float32)
    tanh_val = jnp.tanh(pre_act)
    squash = tanh_val.astype(jnp.bfloat16)
    slope = 1.0 - tanh_val * tanh_val
    branch_part = jnp.einsum("bh,sch->sbc", squash, w_out, preferred_element_type=jnp.float32)
    branch_part = jnp.take(branch_part, back, axis=0, mode="clip")
    start_p = probes.reshape(probes.shape[0], probes.shape[1], n, -1)
    start_p = jnp.take(start_p, order, axis=2, mode="clip")
    running, branch = series(start_p, w_in, w_out, slope, branch_part)
    flowed = u_slice.astype(jnp.float32) + branch
    logdet = running / PROBES
    return (flowed, logdet)


def solution(mesh):
    in_specs = (
        P("dp", None),
        P(None, "tensor"),
        P("tensor", None),
        P("dp", "tensor"),
        P("dp", "tensor"),
        P("dp", "tensor"),
        P(None, "dp", None),
    )
    out_specs = (P("dp", "tensor"), P("dp"))
    return jax.shard_map(local, mesh=mesh, in_specs=in_specs, out_specs=out_specs, check_vma=False)
```

```python
import jax
import jax.numpy as jnp
from jax import lax
from jax.sharding import PartitionSpec as P

L = 4096
PROBES = 2
TERMS = 3


def gather_dp(block):
    n = lax.axis_size("dp")
    ny = n // 2

    def perm(fn):
        return [(d, fn(d // 2, d % 2)) for d in range(n)]

    up = perm(lambda y, c: 2 * ((y + 1) % ny) + c)
    down = perm(lambda y, c: 2 * ((y - 1) % ny) + c)
    swap = perm(lambda y, c: 2 * y + 1 - c)
    fwd = perm(lambda y, c: 2 * ((y + 1) % ny) if c == 0 else 2 * ((y - 1) % ny) + 1)
    fwd_cross = perm(lambda y, c: 2 * ((y + 1) % ny) + 1 if c == 0 else 2 * ((y - 1) % ny))

    from_below = lax.ppermute(block, "dp", up)
    from_above = lax.ppermute(block, "dp", down)
    partner = lax.ppermute(block, "dp", swap)
    d = lax.axis_index("dp")
    y, c = d // 2, d % 2
    relay = jnp.where(c == 0, from_below, from_above)
    far = lax.ppermute(relay, "dp", fwd)
    partner_near = lax.ppermute(jnp.stack([from_below, from_above]), "dp", swap)
    partner_far = lax.ppermute(relay, "dp", fwd_cross)
    joined = jnp.concatenate(
        [block, partner, from_below, from_above, far, partner_near[0], partner_near[1], partner_far]
    )
    rel_y = jnp.array([0, 0, -1, 1, 2, -1, 1, 2], jnp.int32)
    flip = jnp.array([0, 1, 0, 0, 0, 1, 1, 1], jnp.int32)
    block_ids = 2 * ((y + rel_y) % ny) + (c ^ flip)
    return joined, block_ids


def reduce_scatter_pieces(pieces):
    received = lax.all_to_all(pieces.astype(jnp.bfloat16), "tensor", 0, 0)
    return jnp.sum(received.astype(jnp.float32), axis=0)


def all_gather_pieces(piece):
    n = lax.axis_size("tensor")
    return lax.all_to_all(jnp.broadcast_to(piece[None], (n,) + piece.shape), "tensor", 0, 0)


def psum_groups(value):
    n = lax.axis_size("tensor")
    step = 1
    while step < n:
        others = [lax.ppermute(value, "tensor", [(t, t ^ (k * step)) for t in range(n)]) for k in (1, 2, 3)]
        value = (value + others[0]) + (others[1] + others[2])
        step *= 4
    return value


def series(start_p, w_in_p, w_out_p, slope, side):
    t = lax.axis_index("tensor")
    pulled = jnp.einsum("pbsc,sch->pbh", start_p, w_out_p, preferred_element_type=jnp.float32)
    scaled = (pulled * slope[None]).astype(jnp.bfloat16)
    part_u = jnp.einsum("pbh,sch->spbc", scaled, w_in_p, preferred_element_type=jnp.float32)
    pushed = jnp.einsum("pbsc,sch->pbh", start_p, w_in_p, preferred_element_type=jnp.float32)
    scaled_t = (pushed * slope[None]).astype(jnp.bfloat16)
    part_v = jnp.einsum("pbh,sch->spbc", scaled_t, w_out_p, preferred_element_type=jnp.float32)
    summed = reduce_scatter_pieces(jnp.concatenate([part_u, part_v, side[:, None]], axis=1))
    probes_n = start_p.shape[0]
    uv_here = summed[: 2 * probes_n].astype(jnp.bfloat16)
    side = summed[2 * probes_n]
    u_here = uv_here[:probes_n].astype(jnp.float32)
    v_here = uv_here[probes_n:].astype(jnp.float32)
    uv_pieces = all_gather_pieces(uv_here)
    start_here = lax.dynamic_index_in_dim(start_p, t, axis=2, keepdims=False).astype(jnp.float32)
    first = jnp.sum(start_here * u_here, axis=(0, 2))
    second = jnp.sum(v_here * u_here, axis=(0, 2))
    pulled3 = jnp.einsum(
        "spbc,sch->pbh", uv_pieces[:, :probes_n], w_out_p, preferred_element_type=jnp.float32
    )
    scaled3 = (pulled3 * slope[None]).astype(jnp.bfloat16)
    part3 = jnp.einsum("pbh,sch->spbc", scaled3, w_in_p, preferred_element_type=jnp.float32)
    third = jnp.sum(uv_pieces[:, probes_n:].astype(jnp.float32) * part3, axis=(0, 1, 3))
    coeffs = [(-1.0) ** k / (k + 1) for k in range(TERMS)]
    local_sum = coeffs[0] * first + coeffs[1] * second + coeffs[2] * third
    return psum_groups(local_sum), side


def local(features, enc_in, enc_out, noise, in_weight, out_weight, probes):
    n = lax.axis_size("tensor")
    w_in, block_ids = gather_dp(in_weight)
    w_out, _ = gather_dp(out_weight)
    w_in = w_in.reshape(n, -1, in_weight.shape[-1])
    w_out = w_out.reshape(n, -1, out_weight.shape[-1])
    halves = n // block_ids.shape[0]
    order = (halves * block_ids[:, None] + jnp.arange(halves)[None, :]).reshape(-1)
    back = jnp.argsort(order)
    hidden = jax.nn.silu(jnp.dot(features, enc_in, preferred_element_type=jnp.float32)).astype(
        jnp.bfloat16
    )
    enc_out_p = enc_out.reshape(enc_out.shape[0], 2, n, -1)
    stats_p = jnp.einsum("bk,kmsc->sbmc", hidden, enc_out_p, preferred_element_type=jnp.float32)
    moments = reduce_scatter_pieces(stats_p)
    u_slice = (moments[:, 0] + jax.nn.softplus(moments[:, 1]) * noise.astype(jnp.float32)).astype(
        jnp.bfloat16
    )
    u_pieces = jnp.take(all_gather_pieces(u_slice), order, axis=0, mode="clip")
    pre_act = jnp.einsum("sbc,sch->bh", u_pieces, w_in, preferred_element_type=jnp.float32)
    tanh_val = jnp.tanh(pre_act)
    squash = tanh_val.astype(jnp.bfloat16)
    slope = 1.0 - tanh_val * tanh_val
    branch_part = jnp.einsum("bh,sch->sbc", squash, w_out, preferred_element_type=jnp.float32)
    branch_part = jnp.take(branch_part, back, axis=0, mode="clip")
    start_p = probes.reshape(probes.shape[0], probes.shape[1], n, -1)
    start_p = jnp.take(start_p, order, axis=2, mode="clip")
    running, branch = series(start_p, w_in, w_out, slope, branch_part)
    flowed = u_slice.astype(jnp.float32) + branch
    logdet = running / PROBES
    return (flowed, logdet)


def solution(mesh):
    in_specs = (
        P("dp", None),
        P(None, "tensor"),
        P("tensor", None),
        P("dp", "tensor"),
        P("dp", "tensor"),
        P("dp", "tensor"),
        P(None, "dp", None),
    )
    out_specs = (P("dp", "tensor"), P("dp"))
    return jax.shard_map(local, mesh=mesh, in_specs=in_specs, out_specs=out_specs, check_vma=False)
```

```python
import jax
import jax.numpy as jnp
from jax import lax
from jax.sharding import PartitionSpec as P

L = 4096
PROBES = 2
TERMS = 3


def gather_dp(block):
    n = lax.axis_size("dp")
    ny = n // 2

    def perm(fn):
        return [(d, fn(d // 2, d % 2)) for d in range(n)]

    up = perm(lambda y, c: 2 * ((y + 1) % ny) + c)
    down = perm(lambda y, c: 2 * ((y - 1) % ny) + c)
    swap = perm(lambda y, c: 2 * y + 1 - c)
    fwd = perm(lambda y, c: 2 * ((y + 1) % ny) if c == 0 else 2 * ((y - 1) % ny) + 1)

    from_below = lax.ppermute(block, "dp", up)
    from_above = lax.ppermute(block, "dp", down)
    partner = lax.ppermute(block, "dp", swap)
    d = lax.axis_index("dp")
    y, c = d // 2, d % 2
    relay = jnp.where(c == 0, from_below, from_above)
    far = lax.ppermute(relay, "dp", fwd)
    partner_near = [lax.ppermute(from_below, "dp", swap), lax.ppermute(from_above, "dp", swap)]
    partner_far = lax.ppermute(far, "dp", swap)
    joined = jnp.concatenate(
        [block, partner, from_below, from_above, far, partner_near[0], partner_near[1], partner_far]
    )
    rel_y = jnp.array([0, 0, -1, 1, 2, -1, 1, 2], jnp.int32)
    flip = jnp.array([0, 1, 0, 0, 0, 1, 1, 1], jnp.int32)
    block_ids = 2 * ((y + rel_y) % ny) + (c ^ flip)
    return joined, block_ids


def reduce_scatter_pieces(pieces):
    received = lax.all_to_all(pieces.astype(jnp.bfloat16), "tensor", 0, 0)
    return jnp.sum(received.astype(jnp.float32), axis=0)


def all_gather_pieces(piece):
    n = lax.axis_size("tensor")
    return lax.all_to_all(jnp.broadcast_to(piece[None], (n,) + piece.shape), "tensor", 0, 0)


def psum_a2a(value):
    n = lax.axis_size("tensor")
    received = lax.all_to_all(jnp.broadcast_to(value[None], (n,) + value.shape), "tensor", 0, 0)
    return jnp.sum(received, axis=0)


def series(start_p, w_in_p, w_out_p, slope, side):
    t = lax.axis_index("tensor")
    pulled = jnp.einsum("pbsc,sch->pbh", start_p, w_out_p, preferred_element_type=jnp.float32)
    scaled = (pulled * slope[None]).astype(jnp.bfloat16)
    part_u = jnp.einsum("pbh,sch->spbc", scaled, w_in_p, preferred_element_type=jnp.float32)
    pushed = jnp.einsum("pbsc,sch->pbh", start_p, w_in_p, preferred_element_type=jnp.float32)
    scaled_t = (pushed * slope[None]).astype(jnp.bfloat16)
    part_v = jnp.einsum("pbh,sch->spbc", scaled_t, w_out_p, preferred_element_type=jnp.float32)
    summed = reduce_scatter_pieces(jnp.concatenate([part_u, part_v, side[:, None]], axis=1))
    probes_n = start_p.shape[0]
    uv_here = summed[: 2 * probes_n].astype(jnp.bfloat16)
    side = summed[2 * probes_n]
    u_here = uv_here[:probes_n].astype(jnp.float32)
    v_here = uv_here[probes_n:].astype(jnp.float32)
    uv_pieces = all_gather_pieces(uv_here)
    start_here = lax.dynamic_index_in_dim(start_p, t, axis=2, keepdims=False).astype(jnp.float32)
    first = jnp.sum(start_here * u_here, axis=(0, 2))
    second = jnp.sum(v_here * u_here, axis=(0, 2))
    pulled3 = jnp.einsum(
        "spbc,sch->pbh", uv_pieces[:, :probes_n], w_out_p, preferred_element_type=jnp.float32
    )
    scaled3 = (pulled3 * slope[None]).astype(jnp.bfloat16)
    part3 = jnp.einsum("pbh,sch->spbc", scaled3, w_in_p, preferred_element_type=jnp.float32)
    third = jnp.sum(uv_pieces[:, probes_n:].astype(jnp.float32) * part3, axis=(0, 1, 3))
    coeffs = [(-1.0) ** k / (k + 1) for k in range(TERMS)]
    local_sum = coeffs[0] * first + coeffs[1] * second + coeffs[2] * third
    return psum_a2a(local_sum), side


def local(features, enc_in, enc_out, noise, in_weight, out_weight, probes):
    n = lax.axis_size("tensor")
    w_in, block_ids = gather_dp(in_weight)
    w_out, _ = gather_dp(out_weight)
    w_in = w_in.reshape(n, -1, in_weight.shape[-1])
    w_out = w_out.reshape(n, -1, out_weight.shape[-1])
    halves = n // block_ids.shape[0]
    order = (halves * block_ids[:, None] + jnp.arange(halves)[None, :]).reshape(-1)
    back = jnp.argsort(order)
    hidden = jax.nn.silu(jnp.dot(features, enc_in, preferred_element_type=jnp.float32)).astype(
        jnp.bfloat16
    )
    enc_out_p = enc_out.reshape(enc_out.shape[0], 2, n, -1)
    stats_p = jnp.einsum("bk,kmsc->sbmc", hidden, enc_out_p, preferred_element_type=jnp.float32)
    moments = reduce_scatter_pieces(stats_p)
    u_slice = (moments[:, 0] + jax.nn.softplus(moments[:, 1]) * noise.astype(jnp.float32)).astype(
        jnp.bfloat16
    )
    u_pieces = jnp.take(all_gather_pieces(u_slice), order, axis=0, mode="clip")
    pre_act = jnp.einsum("sbc,sch->bh", u_pieces, w_in, preferred_element_type=jnp.float32)
    tanh_val = jnp.tanh(pre_act)
    squash = tanh_val.astype(jnp.bfloat16)
    slope = 1.0 - tanh_val * tanh_val
    branch_part = jnp.einsum("bh,sch->sbc", squash, w_out, preferred_element_type=jnp.float32)
    branch_part = jnp.take(branch_part, back, axis=0, mode="clip")
    start_p = probes.reshape(probes.shape[0], probes.shape[1], n, -1)
    start_p = jnp.take(start_p, order, axis=2, mode="clip")
    running, branch = series(start_p, w_in, w_out, slope, branch_part)
    flowed = u_slice.astype(jnp.float32) + branch
    logdet = running / PROBES
    return (flowed, logdet)


def solution(mesh):
    in_specs = (
        P("dp", None),
        P(None, "tensor"),
        P("tensor", None),
        P("dp", "tensor"),
        P("dp", "tensor"),
        P("dp", "tensor"),
        P(None, "dp", None),
    )
    out_specs = (P("dp", "tensor"), P("dp"))
    return jax.shard_map(local, mesh=mesh, in_specs=in_specs, out_specs=out_specs, check_vma=False)
```

```python
import jax
import jax.numpy as jnp
from jax import lax
from jax.sharding import PartitionSpec as P

L = 4096
PROBES = 2
TERMS = 3


def gather_dp(block):
    n = lax.axis_size("dp")
    ny = n // 2

    def perm(fn):
        return [(d, fn(d // 2, d % 2)) for d in range(n)]

    up = perm(lambda y, c: 2 * ((y + 1) % ny) + c)
    down = perm(lambda y, c: 2 * ((y - 1) % ny) + c)
    swap = perm(lambda y, c: 2 * y + 1 - c)
    fwd = perm(lambda y, c: 2 * ((y + 1) % ny) if c == 0 else 2 * ((y - 1) % ny) + 1)

    from_below = lax.ppermute(block, "dp", up)
    from_above = lax.ppermute(block, "dp", down)
    partner = lax.ppermute(block, "dp", swap)
    d = lax.axis_index("dp")
    y, c = d // 2, d % 2
    relay = jnp.where(c == 0, from_below, from_above)
    far = lax.ppermute(relay, "dp", fwd)
    partner_near = lax.ppermute(jnp.stack([from_below, from_above]), "dp", swap)
    partner_far = lax.ppermute(far, "dp", swap)
    joined = jnp.stack(
        [block, partner, from_below, from_above, far, partner_near[0], partner_near[1], partner_far], axis=1
    )
    rel_y = jnp.array([0, 0, -1, 1, 2, -1, 1, 2], jnp.int32)
    flip = jnp.array([0, 1, 0, 0, 0, 1, 1, 1], jnp.int32)
    block_ids = 2 * ((y + rel_y) % ny) + (c ^ flip)
    return joined, block_ids


def reduce_scatter_pieces(pieces):
    received = lax.all_to_all(pieces.astype(jnp.bfloat16), "tensor", 0, 0)
    return jnp.sum(received.astype(jnp.float32), axis=0)


def all_gather_pieces(piece):
    n = lax.axis_size("tensor")
    return lax.all_to_all(jnp.broadcast_to(piece[None], (n,) + piece.shape), "tensor", 0, 0)


def psum_groups(value):
    n = lax.axis_size("tensor")
    step = 1
    while step < n:
        others = [lax.ppermute(value, "tensor", [(t, t ^ (k * step)) for t in range(n)]) for k in (1, 2, 3)]
        value = (value + others[0]) + (others[1] + others[2])
        step *= 4
    return value


def series(start_p, w_in_p, w_out_p, slope, side):
    t = lax.axis_index("tensor")
    pulled = jnp.einsum("pbsc,sch->pbh", start_p, w_out_p, preferred_element_type=jnp.float32)
    scaled = (pulled * slope[None]).astype(jnp.bfloat16)
    part_u = jnp.einsum("pbh,sch->spbc", scaled, w_in_p, preferred_element_type=jnp.float32)
    pushed = jnp.einsum("pbsc,sch->pbh", start_p, w_in_p, preferred_element_type=jnp.float32)
    scaled_t = (pushed * slope[None]).astype(jnp.bfloat16)
    part_v = jnp.einsum("pbh,sch->spbc", scaled_t, w_out_p, preferred_element_type=jnp.float32)
    summed = reduce_scatter_pieces(jnp.concatenate([part_u, part_v, side[:, None]], axis=1))
    probes_n = start_p.shape[0]
    uv_here = summed[: 2 * probes_n].astype(jnp.bfloat16)
    side = summed[2 * probes_n]
    u_here = uv_here[:probes_n].astype(jnp.float32)
    v_here = uv_here[probes_n:].astype(jnp.float32)
    uv_pieces = all_gather_pieces(uv_here)
    start_here = lax.dynamic_index_in_dim(start_p, t, axis=2, keepdims=False).astype(jnp.float32)
    first = jnp.sum(start_here * u_here, axis=(0, 2))
    second = jnp.sum(v_here * u_here, axis=(0, 2))
    pulled3 = jnp.einsum(
        "spbc,sch->pbh", uv_pieces[:, :probes_n], w_out_p, preferred_element_type=jnp.float32
    )
    scaled3 = (pulled3 * slope[None]).astype(jnp.bfloat16)
    part3 = jnp.einsum("pbh,sch->spbc", scaled3, w_in_p, preferred_element_type=jnp.float32)
    third = jnp.sum(uv_pieces[:, probes_n:].astype(jnp.float32) * part3, axis=(0, 1, 3))
    coeffs = [(-1.0) ** k / (k + 1) for k in range(TERMS)]
    local_sum = coeffs[0] * first + coeffs[1] * second + coeffs[2] * third
    return psum_groups(local_sum), side


def local(features, enc_in, enc_out, noise, in_weight, out_weight, probes):
    n = lax.axis_size("tensor")
    both, block_ids = gather_dp(jnp.stack([in_weight, out_weight]))
    w_in = both[0].reshape(n, -1, in_weight.shape[-1])
    w_out = both[1].reshape(n, -1, out_weight.shape[-1])
    halves = n // block_ids.shape[0]
    order = (halves * block_ids[:, None] + jnp.arange(halves)[None, :]).reshape(-1)
    back = jnp.argsort(order)
    hidden = jax.nn.silu(jnp.dot(features, enc_in, preferred_element_type=jnp.float32)).astype(
        jnp.bfloat16
    )
    enc_out_p = enc_out.reshape(enc_out.shape[0], 2, n, -1)
    stats_p = jnp.einsum("bk,kmsc->sbmc", hidden, enc_out_p, preferred_element_type=jnp.float32)
    moments = reduce_scatter_pieces(stats_p)
    u_slice = (moments[:, 0] + jax.nn.softplus(moments[:, 1]) * noise.astype(jnp.float32)).astype(
        jnp.bfloat16
    )
    u_pieces = jnp.take(all_gather_pieces(u_slice), order, axis=0, mode="clip")
    pre_act = jnp.einsum("sbc,sch->bh", u_pieces, w_in, preferred_element_type=jnp.float32)
    tanh_val = jnp.tanh(pre_act)
    squash = tanh_val.astype(jnp.bfloat16)
    slope = 1.0 - tanh_val * tanh_val
    branch_part = jnp.einsum("bh,sch->sbc", squash, w_out, preferred_element_type=jnp.float32)
    branch_part = jnp.take(branch_part, back, axis=0, mode="clip")
    start_p = probes.reshape(probes.shape[0], probes.shape[1], n, -1)
    start_p = jnp.take(start_p, order, axis=2, mode="clip")
    running, branch = series(start_p, w_in, w_out, slope, branch_part)
    flowed = u_slice.astype(jnp.float32) + branch
    logdet = running / PROBES
    return (flowed, logdet)


def solution(mesh):
    in_specs = (
        P("dp", None),
        P(None, "tensor"),
        P("tensor", None),
        P("dp", "tensor"),
        P("dp", "tensor"),
        P("dp", "tensor"),
        P(None, "dp", None),
    )
    out_specs = (P("dp", "tensor"), P("dp"))
    return jax.shard_map(local, mesh=mesh, in_specs=in_specs, out_specs=out_specs, check_vma=False)
```

```python
import jax
import jax.numpy as jnp
from jax import lax
from jax.sharding import PartitionSpec as P

L = 4096
PROBES = 2
TERMS = 3


def gather_dp(block):
    n = lax.axis_size("dp")
    ny = n // 2

    def perm(fn):
        return [(d, fn(d // 2, d % 2)) for d in range(n)]

    up = perm(lambda y, c: 2 * ((y + 1) % ny) + c)
    down = perm(lambda y, c: 2 * ((y - 1) % ny) + c)
    swap = perm(lambda y, c: 2 * y + 1 - c)
    fwd = perm(lambda y, c: 2 * ((y + 1) % ny) if c == 0 else 2 * ((y - 1) % ny) + 1)

    from_below = lax.ppermute(block, "dp", up)
    from_above = lax.ppermute(block, "dp", down)
    partner = lax.ppermute(block, "dp", swap)
    d = lax.axis_index("dp")
    y, c = d // 2, d % 2
    relay = jnp.where(c == 0, from_below, from_above)
    far = lax.ppermute(relay, "dp", fwd)
    partner_near = lax.ppermute(jnp.stack([from_below, from_above]), "dp", swap)
    partner_far = lax.ppermute(far, "dp", swap)
    joined = jnp.concatenate(
        [block, partner, from_below, from_above, far, partner_near[0], partner_near[1], partner_far]
    )
    rel_y = jnp.array([0, 0, -1, 1, 2, -1, 1, 2], jnp.int32)
    flip = jnp.array([0, 1, 0, 0, 0, 1, 1, 1], jnp.int32)
    block_ids = 2 * ((y + rel_y) % ny) + (c ^ flip)
    return joined, block_ids


def reduce_scatter_pieces(pieces):
    received = lax.all_to_all(pieces.astype(jnp.bfloat16), "tensor", 0, 0)
    return jnp.sum(received.astype(jnp.float32), axis=0)


def all_gather_pieces(piece):
    n = lax.axis_size("tensor")
    return lax.all_to_all(jnp.broadcast_to(piece[None], (n,) + piece.shape), "tensor", 0, 0)


def psum_a2a(value):
    n = lax.axis_size("tensor")
    received = lax.all_to_all(jnp.broadcast_to(value[None], (n,) + value.shape), "tensor", 0, 0)
    return jnp.sum(received, axis=0)


def series(start_p, w_in_p, w_out_p, slope, side):
    t = lax.axis_index("tensor")
    pulled = jnp.einsum("pbsc,sch->pbh", start_p, w_out_p, preferred_element_type=jnp.float32)
    scaled = (pulled * slope[None]).astype(jnp.bfloat16)
    part_u = jnp.einsum("pbh,sch->spbc", scaled, w_in_p, preferred_element_type=jnp.float32)
    pushed = jnp.einsum("pbsc,sch->pbh", start_p, w_in_p, preferred_element_type=jnp.float32)
    scaled_t = (pushed * slope[None]).astype(jnp.bfloat16)
    part_v = jnp.einsum("pbh,sch->spbc", scaled_t, w_out_p, preferred_element_type=jnp.float32)
    summed = reduce_scatter_pieces(jnp.concatenate([part_u, part_v, side[:, None]], axis=1))
    probes_n = start_p.shape[0]
    uv_here = summed[: 2 * probes_n].astype(jnp.bfloat16)
    side = summed[2 * probes_n]
    u_here = uv_here[:probes_n].astype(jnp.float32)
    v_here = uv_here[probes_n:].astype(jnp.float32)
    uv_pieces = all_gather_pieces(uv_here)
    start_here = lax.dynamic_index_in_dim(start_p, t, axis=2, keepdims=False).astype(jnp.float32)
    first = jnp.sum(start_here * u_here, axis=(0, 2))
    second = jnp.sum(v_here * u_here, axis=(0, 2))
    pulled3 = jnp.einsum(
        "spbc,sch->pbh", uv_pieces[:, :probes_n], w_out_p, preferred_element_type=jnp.float32
    )
    scaled3 = (pulled3 * slope[None]).astype(jnp.bfloat16)
    part3 = jnp.einsum("pbh,sch->spbc", scaled3, w_in_p, preferred_element_type=jnp.float32)
    third = jnp.sum(uv_pieces[:, probes_n:].astype(jnp.float32) * part3, axis=(0, 1, 3))
    coeffs = [(-1.0) ** k / (k + 1) for k in range(TERMS)]
    local_sum = coeffs[0] * first + coeffs[1] * second + coeffs[2] * third
    return psum_a2a(local_sum), side


def local(features, enc_in, enc_out, noise, in_weight, out_weight, probes):
    n = lax.axis_size("tensor")
    w_in, block_ids = gather_dp(in_weight)
    w_out, _ = gather_dp(out_weight)
    w_in = w_in.reshape(n, -1, in_weight.shape[-1])
    w_out = w_out.reshape(n, -1, out_weight.shape[-1])
    halves = n // block_ids.shape[0]
    order = (halves * block_ids[:, None] + jnp.arange(halves)[None, :]).reshape(-1)
    back = jnp.argsort(order)
    hidden = jax.nn.silu(jnp.dot(features, enc_in, preferred_element_type=jnp.float32)).astype(
        jnp.bfloat16
    )
    enc_out_p = enc_out.reshape(enc_out.shape[0], 2, n, -1)
    stats_p = jnp.einsum("bk,kmsc->sbmc", hidden, enc_out_p, preferred_element_type=jnp.float32)
    moments = reduce_scatter_pieces(stats_p)
    u_slice = (moments[:, 0] + jax.nn.softplus(moments[:, 1]) * noise.astype(jnp.float32)).astype(
        jnp.bfloat16
    )
    u_pieces = jnp.take(all_gather_pieces(u_slice), order, axis=0, mode="clip")
    pre_act = jnp.einsum("sbc,sch->bh", u_pieces, w_in, preferred_element_type=jnp.float32)
    tanh_val = jnp.tanh(pre_act)
    squash = tanh_val.astype(jnp.bfloat16)
    slope = 1.0 - tanh_val * tanh_val
    branch_part = jnp.einsum("bh,sch->sbc", squash, w_out, preferred_element_type=jnp.float32)
    branch_part = jnp.take(branch_part, back, axis=0, mode="clip")
    start_p = probes.reshape(probes.shape[0], probes.shape[1], n, -1)
    start_p = jnp.take(start_p, order, axis=2, mode="clip")
    running, branch = series(start_p, w_in, w_out, slope, branch_part)
    flowed = u_slice.astype(jnp.float32) + branch
    logdet = running / PROBES
    return (flowed, logdet)


def solution(mesh):
    in_specs = (
        P("dp", None),
        P(None, "tensor"),
        P("tensor", None),
        P("dp", "tensor"),
        P("dp", "tensor"),
        P("dp", "tensor"),
        P(None, "dp", None),
    )
    out_specs = (P("dp", "tensor"), P("dp"))
    return jax.shard_map(local, mesh=mesh, in_specs=in_specs, out_specs=out_specs, check_vma=False)
```

```python
import jax
import jax.numpy as jnp
from jax import lax
from jax.sharding import PartitionSpec as P

L = 4096
PROBES = 2
TERMS = 3


def gather_dp(block):
    n = lax.axis_size("dp")
    ny = n // 2

    def perm(fn):
        return [(d, fn(d // 2, d % 2)) for d in range(n)]

    up = perm(lambda y, c: 2 * ((y + 1) % ny) + c)
    down = perm(lambda y, c: 2 * ((y - 1) % ny) + c)
    swap = perm(lambda y, c: 2 * y + 1 - c)
    fwd = perm(lambda y, c: 2 * ((y + 1) % ny) if c == 0 else 2 * ((y - 1) % ny) + 1)

    from_below = lax.ppermute(block, "dp", up)
    from_above = lax.ppermute(block, "dp", down)
    partner = lax.ppermute(block, "dp", swap)
    d = lax.axis_index("dp")
    y, c = d // 2, d % 2
    relay = jnp.where(c == 0, from_below, from_above)
    far = lax.ppermute(relay, "dp", fwd)
    partner_near = lax.ppermute(jnp.stack([from_below, from_above]), "dp", swap)
    partner_far = lax.ppermute(far, "dp", swap)
    joined = jnp.concatenate(
        [block, partner, from_below, from_above, far, partner_near[0], partner_near[1], partner_far]
    )
    rel_y = jnp.array([0, 0, -1, 1, 2, -1, 1, 2], jnp.int32)
    flip = jnp.array([0, 1, 0, 0, 0, 1, 1, 1], jnp.int32)
    block_ids = 2 * ((y + rel_y) % ny) + (c ^ flip)
    return joined, block_ids


def reduce_scatter_pieces(pieces):
    received = lax.all_to_all(pieces.astype(jnp.bfloat16), "tensor", 0, 0)
    return jnp.sum(received.astype(jnp.float32), axis=0)


def all_gather_pieces(piece):
    n = lax.axis_size("tensor")
    return lax.all_to_all(jnp.broadcast_to(piece[None], (n,) + piece.shape), "tensor", 0, 0)


def psum_a2a(value):
    n = lax.axis_size("tensor")
    received = lax.all_to_all(jnp.broadcast_to(value[None], (n,) + value.shape), "tensor", 0, 0)
    return jnp.sum(received, axis=0)


def series(start_p, order, w_in_p, w_out_p, slope, squash, pushed):
    t = lax.axis_index("tensor")
    pulled = jnp.einsum("pbsc,sch->pbh", start_p, w_out_p, preferred_element_type=jnp.float32)
    scaled = (pulled * slope[None]).astype(jnp.bfloat16)
    part_u = jnp.einsum("pbh,sch->spbc", scaled, w_in_p, preferred_element_type=jnp.float32)
    scaled_t = (pushed * slope[None]).astype(jnp.bfloat16)
    rows_in = jnp.concatenate([squash[None], scaled_t], axis=0)
    rows_out = jnp.einsum("pbh,sch->spbc", rows_in, w_out_p, preferred_element_type=jnp.float32)
    side, part_v = rows_out[:, 0], rows_out[:, 1:]
    side = jnp.take(side, jnp.argsort(order), axis=0, mode="clip")
    summed = reduce_scatter_pieces(jnp.concatenate([part_u, part_v, side[:, None]], axis=1))
    probes_n = start_p.shape[0]
    uv_here = summed[: 2 * probes_n].astype(jnp.bfloat16)
    side = summed[2 * probes_n]
    u_here = uv_here[:probes_n].astype(jnp.float32)
    v_here = uv_here[probes_n:].astype(jnp.float32)
    uv_pieces = all_gather_pieces(uv_here)
    start_here = lax.dynamic_index_in_dim(start_p, t, axis=2, keepdims=False).astype(jnp.float32)
    first = jnp.sum(start_here * u_here, axis=(0, 2))
    second = jnp.sum(v_here * u_here, axis=(0, 2))
    pulled3 = jnp.einsum(
        "spbc,sch->pbh", uv_pieces[:, :probes_n], w_out_p, preferred_element_type=jnp.float32
    )
    scaled3 = (pulled3 * slope[None]).astype(jnp.bfloat16)
    part3 = jnp.einsum("pbh,sch->spbc", scaled3, w_in_p, preferred_element_type=jnp.float32)
    third = jnp.sum(uv_pieces[:, probes_n:].astype(jnp.float32) * part3, axis=(0, 1, 3))
    coeffs = [(-1.0) ** k / (k + 1) for k in range(TERMS)]
    local_sum = coeffs[0] * first + coeffs[1] * second + coeffs[2] * third
    return psum_a2a(local_sum), side


def local(features, enc_in, enc_out, noise, in_weight, out_weight, probes):
    n = lax.axis_size("tensor")
    w_in, block_ids = gather_dp(in_weight)
    w_out, _ = gather_dp(out_weight)
    w_in = w_in.reshape(n, -1, in_weight.shape[-1])
    w_out = w_out.reshape(n, -1, out_weight.shape[-1])
    halves = n // block_ids.shape[0]
    order = (halves * block_ids[:, None] + jnp.arange(halves)[None, :]).reshape(-1)
    hidden = jax.nn.silu(jnp.dot(features, enc_in, preferred_element_type=jnp.float32)).astype(
        jnp.bfloat16
    )
    enc_out_p = enc_out.reshape(enc_out.shape[0], 2, n, -1)
    stats_p = jnp.einsum("bk,kmsc->sbmc", hidden, enc_out_p, preferred_element_type=jnp.float32)
    moments = reduce_scatter_pieces(stats_p)
    u_slice = (moments[:, 0] + jax.nn.softplus(moments[:, 1]) * noise.astype(jnp.float32)).astype(
        jnp.bfloat16
    )
    u_pieces = jnp.take(all_gather_pieces(u_slice), order, axis=0, mode="clip")
    start_p = probes.reshape(probes.shape[0], probes.shape[1], n, -1)
    start_p = jnp.take(start_p, order, axis=2, mode="clip")
    rows_in = jnp.concatenate([jnp.moveaxis(u_pieces, 1, 0)[None], start_p], axis=0)
    rows_out = jnp.einsum("pbsc,sch->pbh", rows_in, w_in, preferred_element_type=jnp.float32)
    pre_act, pushed = rows_out[0], rows_out[1:]
    tanh_val = jnp.tanh(pre_act)
    squash = tanh_val.astype(jnp.bfloat16)
    slope = 1.0 - tanh_val * tanh_val
    running, branch = series(start_p, order, w_in, w_out, slope, squash, pushed)
    flowed = u_slice.astype(jnp.float32) + branch
    logdet = running / PROBES
    return (flowed, logdet)


def solution(mesh):
    in_specs = (
        P("dp", None),
        P(None, "tensor"),
        P("tensor", None),
        P("dp", "tensor"),
        P("dp", "tensor"),
        P("dp", "tensor"),
        P(None, "dp", None),
    )
    out_specs = (P("dp", "tensor"), P("dp"))
    return jax.shard_map(local, mesh=mesh, in_specs=in_specs, out_specs=out_specs, check_vma=False)
```

```python
import jax
import jax.numpy as jnp
from jax import lax
from jax.sharding import PartitionSpec as P

L = 4096
PROBES = 2
TERMS = 3


def gather_dp(block):
    n = lax.axis_size("dp")
    ny = n // 2

    def perm(fn):
        return [(d, fn(d // 2, d % 2)) for d in range(n)]

    up = perm(lambda y, c: 2 * ((y + 1) % ny) + c)
    down = perm(lambda y, c: 2 * ((y - 1) % ny) + c)
    swap = perm(lambda y, c: 2 * y + 1 - c)
    fwd = perm(lambda y, c: 2 * ((y + 1) % ny) if c == 0 else 2 * ((y - 1) % ny) + 1)

    from_below = lax.ppermute(block, "dp", up)
    from_above = lax.ppermute(block, "dp", down)
    partner = lax.ppermute(block, "dp", swap)
    d = lax.axis_index("dp")
    y, c = d // 2, d % 2
    relay = jnp.where(c == 0, from_below, from_above)
    far = lax.ppermute(relay, "dp", fwd)
    partner_near = lax.ppermute(jnp.stack([from_below, from_above]), "dp", swap)
    partner_far = lax.ppermute(far, "dp", swap)
    joined = jnp.concatenate(
        [block, partner, from_below, from_above, far, partner_near[0], partner_near[1], partner_far]
    )
    rel_y = jnp.array([0, 0, -1, 1, 2, -1, 1, 2], jnp.int32)
    flip = jnp.array([0, 1, 0, 0, 0, 1, 1, 1], jnp.int32)
    block_ids = 2 * ((y + rel_y) % ny) + (c ^ flip)
    return joined, block_ids


def reduce_scatter_pieces(pieces):
    received = lax.all_to_all(pieces.astype(jnp.bfloat16), "tensor", 0, 0)
    return jnp.sum(received.astype(jnp.float32), axis=0)


def all_gather_pieces(piece):
    n = lax.axis_size("tensor")
    return lax.all_to_all(jnp.broadcast_to(piece[None], (n,) + piece.shape), "tensor", 0, 0)


def psum_a2a(value):
    n = lax.axis_size("tensor")
    received = lax.all_to_all(jnp.broadcast_to(value[None], (n,) + value.shape), "tensor", 0, 0)
    return jnp.sum(received, axis=0)


def series(start_p, order, w_in_p, w_out_p, slope, squash, pushed):
    t = lax.axis_index("tensor")
    pulled = jnp.einsum("pbsc,sch->pbh", start_p, w_out_p, preferred_element_type=jnp.float32)
    scaled = (pulled * slope[None]).astype(jnp.bfloat16)
    part_u = jnp.einsum("pbh,sch->spbc", scaled, w_in_p, preferred_element_type=jnp.float32)
    scaled_t = (pushed * slope[None]).astype(jnp.bfloat16)
    rows_in = jnp.concatenate([squash[None], scaled_t], axis=0)
    rows_out = jnp.einsum("pbh,sch->spbc", rows_in, w_out_p, preferred_element_type=jnp.float32)
    side, part_v = rows_out[:, 0], rows_out[:, 1:]
    side = jnp.take(side, jnp.argsort(order), axis=0, mode="clip")
    summed = reduce_scatter_pieces(jnp.concatenate([part_u, part_v, side[:, None]], axis=1))
    probes_n = start_p.shape[0]
    uv_here = summed[: 2 * probes_n].astype(jnp.bfloat16)
    side = summed[2 * probes_n]
    u_here = uv_here[:probes_n].astype(jnp.float32)
    v_here = uv_here[probes_n:].astype(jnp.float32)
    uv_pieces = all_gather_pieces(uv_here)
    start_here = lax.dynamic_index_in_dim(start_p, t, axis=2, keepdims=False).astype(jnp.float32)
    first = jnp.sum(start_here * u_here, axis=(0, 2))
    second = jnp.sum(v_here * u_here, axis=(0, 2))
    pulled3 = jnp.einsum(
        "spbc,sch->pbh", uv_pieces[:, :probes_n], w_out_p, preferred_element_type=jnp.float32
    )
    scaled3 = (pulled3 * slope[None]).astype(jnp.bfloat16)
    part3 = jnp.einsum("pbh,sch->spbc", scaled3, w_in_p, preferred_element_type=jnp.float32)
    third = jnp.sum(uv_pieces[:, probes_n:].astype(jnp.float32) * part3, axis=(0, 1, 3))
    coeffs = [(-1.0) ** k / (k + 1) for k in range(TERMS)]
    local_sum = coeffs[0] * first + coeffs[1] * second + coeffs[2] * third
    return psum_a2a(local_sum), side


def local(features, enc_in, enc_out, noise, in_weight, out_weight, probes):
    n = lax.axis_size("tensor")
    w_in, block_ids = gather_dp(in_weight)
    w_out, _ = gather_dp(out_weight)
    w_in = w_in.reshape(n, -1, in_weight.shape[-1])
    w_out = w_out.reshape(n, -1, out_weight.shape[-1])
    halves = n // block_ids.shape[0]
    order = (halves * block_ids[:, None] + jnp.arange(halves)[None, :]).reshape(-1)
    hidden = jax.nn.silu(jnp.dot(features, enc_in, preferred_element_type=jnp.float32)).astype(
        jnp.bfloat16
    )
    stats = jnp.dot(hidden, enc_out, preferred_element_type=jnp.float32)
    stats = stats.astype(jnp.bfloat16).reshape(stats.shape[0], 2, n, -1)
    received = lax.all_to_all(stats, "tensor", 2, 2)
    moments = jnp.sum(received.astype(jnp.float32), axis=2)
    u_slice = (moments[:, 0] + jax.nn.softplus(moments[:, 1]) * noise.astype(jnp.float32)).astype(
        jnp.bfloat16
    )
    u_pieces = jnp.take(all_gather_pieces(u_slice), order, axis=0, mode="clip")
    start_p = probes.reshape(probes.shape[0], probes.shape[1], n, -1)
    start_p = jnp.take(start_p, order, axis=2, mode="clip")
    rows_in = jnp.concatenate([jnp.moveaxis(u_pieces, 1, 0)[None], start_p], axis=0)
    rows_out = jnp.einsum("pbsc,sch->pbh", rows_in, w_in, preferred_element_type=jnp.float32)
    pre_act, pushed = rows_out[0], rows_out[1:]
    tanh_val = jnp.tanh(pre_act)
    squash = tanh_val.astype(jnp.bfloat16)
    slope = 1.0 - tanh_val * tanh_val
    running, branch = series(start_p, order, w_in, w_out, slope, squash, pushed)
    flowed = u_slice.astype(jnp.float32) + branch
    logdet = running / PROBES
    return (flowed, logdet)


def solution(mesh):
    in_specs = (
        P("dp", None),
        P(None, "tensor"),
        P("tensor", None),
        P("dp", "tensor"),
        P("dp", "tensor"),
        P("dp", "tensor"),
        P(None, "dp", None),
    )
    out_specs = (P("dp", "tensor"), P("dp"))
    return jax.shard_map(local, mesh=mesh, in_specs=in_specs, out_specs=out_specs, check_vma=False)
```

```python
import jax
import jax.numpy as jnp
from jax import lax
from jax.sharding import PartitionSpec as P

L = 4096
PROBES = 2
TERMS = 3


def gather_dp(block):
    n = lax.axis_size("dp")
    ny = n // 2

    def perm(fn):
        return [(d, fn(d // 2, d % 2)) for d in range(n)]

    up = perm(lambda y, c: 2 * ((y + 1) % ny) + c)
    down = perm(lambda y, c: 2 * ((y - 1) % ny) + c)
    swap = perm(lambda y, c: 2 * y + 1 - c)
    fwd = perm(lambda y, c: 2 * ((y + 1) % ny) if c == 0 else 2 * ((y - 1) % ny) + 1)

    from_below = lax.ppermute(block, "dp", up)
    from_above = lax.ppermute(block, "dp", down)
    partner = lax.ppermute(block, "dp", swap)
    d = lax.axis_index("dp")
    y, c = d // 2, d % 2
    relay = jnp.where(c == 0, from_below, from_above)
    far = lax.ppermute(relay, "dp", fwd)
    partner_near = lax.ppermute(jnp.stack([from_below, from_above]), "dp", swap)
    partner_far = lax.ppermute(far, "dp", swap)
    joined = jnp.concatenate(
        [block, partner, from_below, from_above, far, partner_near[0], partner_near[1], partner_far]
    )
    rel_y = jnp.array([0, 0, -1, 1, 2, -1, 1, 2], jnp.int32)
    flip = jnp.array([0, 1, 0, 0, 0, 1, 1, 1], jnp.int32)
    block_ids = 2 * ((y + rel_y) % ny) + (c ^ flip)
    return joined, block_ids


def reduce_scatter_pieces(pieces):
    received = lax.all_to_all(pieces.astype(jnp.bfloat16), "tensor", 0, 0)
    return jnp.sum(received.astype(jnp.float32), axis=0)


def all_gather_pieces(piece):
    n = lax.axis_size("tensor")
    return lax.all_to_all(jnp.broadcast_to(piece[None], (n,) + piece.shape), "tensor", 0, 0)


def psum_a2a(value):
    n = lax.axis_size("tensor")
    received = lax.all_to_all(jnp.broadcast_to(value[None], (n,) + value.shape), "tensor", 0, 0)
    return jnp.sum(received, axis=0)


def series(start_p, order, w_in_p, w_out_p, slope, squash, pushed):
    t = lax.axis_index("tensor")
    pulled = jnp.einsum("pbsc,sch->pbh", start_p, w_out_p, preferred_element_type=jnp.float32)
    scaled = (pulled * slope[None]).astype(jnp.bfloat16)
    part_u = jnp.einsum("pbh,sch->spbc", scaled, w_in_p, preferred_element_type=jnp.float32)
    scaled_t = (pushed * slope[None]).astype(jnp.bfloat16)
    rows_in = jnp.concatenate([squash[None], scaled_t], axis=0)
    rows_out = jnp.einsum("pbh,sch->spbc", rows_in, w_out_p, preferred_element_type=jnp.float32)
    side, part_v = rows_out[:, 0], rows_out[:, 1:]
    side = jnp.take(side, jnp.argsort(order), axis=0, mode="clip")
    summed = reduce_scatter_pieces(jnp.concatenate([part_u, part_v, side[:, None]], axis=1))
    probes_n = start_p.shape[0]
    uv_here = summed[: 2 * probes_n].astype(jnp.bfloat16)
    side = summed[2 * probes_n]
    u_here = uv_here[:probes_n].astype(jnp.float32)
    v_here = uv_here[probes_n:].astype(jnp.float32)
    uv_pieces = all_gather_pieces(uv_here)
    start_here = lax.dynamic_index_in_dim(start_p, t, axis=2, keepdims=False).astype(jnp.float32)
    first = jnp.sum(start_here * u_here, axis=(0, 2))
    second = jnp.sum(v_here * u_here, axis=(0, 2))
    pulled3 = jnp.einsum(
        "spbc,sch->pbh", uv_pieces[:, :probes_n], w_out_p, preferred_element_type=jnp.float32
    )
    scaled3 = (pulled3 * slope[None]).astype(jnp.bfloat16)
    v_win = jnp.einsum(
        "spbc,sch->pbh", uv_pieces[:, probes_n:], w_in_p, preferred_element_type=jnp.float32
    )
    third = jnp.sum(v_win * scaled3.astype(jnp.float32), axis=(0, 2))
    coeffs = [(-1.0) ** k / (k + 1) for k in range(TERMS)]
    local_sum = coeffs[0] * first + coeffs[1] * second + coeffs[2] * third
    return psum_a2a(local_sum), side


def local(features, enc_in, enc_out, noise, in_weight, out_weight, probes):
    n = lax.axis_size("tensor")
    w_in, block_ids = gather_dp(in_weight)
    w_out, _ = gather_dp(out_weight)
    w_in = w_in.reshape(n, -1, in_weight.shape[-1])
    w_out = w_out.reshape(n, -1, out_weight.shape[-1])
    halves = n // block_ids.shape[0]
    order = (halves * block_ids[:, None] + jnp.arange(halves)[None, :]).reshape(-1)
    hidden = jax.nn.silu(jnp.dot(features, enc_in, preferred_element_type=jnp.float32)).astype(
        jnp.bfloat16
    )
    enc_out_p = enc_out.reshape(enc_out.shape[0], 2, n, -1)
    stats_p = jnp.einsum("bk,kmsc->sbmc", hidden, enc_out_p, preferred_element_type=jnp.float32)
    moments = reduce_scatter_pieces(stats_p)
    u_slice = (moments[:, 0] + jax.nn.softplus(moments[:, 1]) * noise.astype(jnp.float32)).astype(
        jnp.bfloat16
    )
    u_pieces = jnp.take(all_gather_pieces(u_slice), order, axis=0, mode="clip")
    start_p = probes.reshape(probes.shape[0], probes.shape[1], n, -1)
    start_p = jnp.take(start_p, order, axis=2, mode="clip")
    rows_in = jnp.concatenate([jnp.moveaxis(u_pieces, 1, 0)[None], start_p], axis=0)
    rows_out = jnp.einsum("pbsc,sch->pbh", rows_in, w_in, preferred_element_type=jnp.float32)
    pre_act, pushed = rows_out[0], rows_out[1:]
    tanh_val = jnp.tanh(pre_act)
    squash = tanh_val.astype(jnp.bfloat16)
    slope = 1.0 - tanh_val * tanh_val
    running, branch = series(start_p, order, w_in, w_out, slope, squash, pushed)
    flowed = u_slice.astype(jnp.float32) + branch
    logdet = running / PROBES
    return (flowed, logdet)


def solution(mesh):
    in_specs = (
        P("dp", None),
        P(None, "tensor"),
        P("tensor", None),
        P("dp", "tensor"),
        P("dp", "tensor"),
        P("dp", "tensor"),
        P(None, "dp", None),
    )
    out_specs = (P("dp", "tensor"), P("dp"))
    return jax.shard_map(local, mesh=mesh, in_specs=in_specs, out_specs=out_specs, check_vma=False)
```
